512 devices in a mesh: req: 64 (over y, z), tp: 8 (over x, core).
Axes of the slice: x: 4, y: 8, z: 8, core: 2. Of those that a mesh axis runs over, the one named last changes fastest.
Arguments:
- tokens: bfloat16 [16384, 2048], P('req', 'tp'), may hold values from -6 to 6
- norm_gain: float32 [2048], replicated, may hold values from 0.1 to 1.9
- input_weight: bfloat16 [2048, 3, 2048], P(None, None, 'tp'), may hold values from -0.125 to 0.125
- output_weight: bfloat16 [2048, 2048], P('tp'), may hold values from -1 to 1
- cache_store: bfloat16 [64, 2, 512, 2048], P('req', None, None, 'tp'), may hold values from -210 to 210
- cache_length: int32 [64], replicated, may hold values from 1 to 512, 16384 in all
- placement: int32 [64], replicated, may hold values from 0 to 63, each once
- accept: int32 [2, 16384], replicated, may hold values 0 or 1
Outputs:
- first_pass: float32 [16384, 2048], P('req', 'tp')
- final: float32 [16384, 2048], P('req', 'tp')
The draws below stay inside these ranges and needn't reach their ends.
Inputs may be any that keep to these rules, and one draw needn't show every extreme that they name: Request r's cache lies in slot placement[r]; slot s is held by index s of req. The live entries of a request's cache are the first cache_length[r] of its slot. `accept`: 1 marks a block token accepted in that pass.
All inputs are finite; a program needn't handle non-finite values.
Results may differ from the reference program's by a relative error of at most 0.024.
The reference program's roundings to bfloat16 on the way count: a program that leaves them out, or rounds other values in their place, can miss the bound.
Values may be sent and summed in bfloat16 or wider, within the bound.
No kernel may reach another device: no remote copies, remote signals or barrier semaphores. Data moves between devices by JAX's collectives and lax.ppermute only.
A program may use at most 64 MiB of HBM per device.

```python
import math
import jax
import jax.numpy as jnp
import numpy as np
from jax import lax

D = 2048
HEADS = 16
HD = 128
BLOCK = 256
CMAX = 512
REQS = 64


def draw_cache_store(key, part):
    shape = (REQS, 2, CMAX, HEADS * HD)
    entries = jnp.clip(jax.random.normal(key, shape, jnp.float32), -6.0, 6.0)
    return entries.astype(jnp.bfloat16)


def touch_ends(values, rng, low, largest):
    shape = values.shape
    index_at = [jax.random.randint(jax.random.fold_in(rng, axis), (), 0, shape[axis]) for axis in range(len(shape))]
    values = values.at[tuple(index_at)].set(low)
    longest = shape.index(max(shape))
    index_at[longest] = (index_at[longest] + 1) % shape[longest]
    return values.at[tuple(index_at)].set(largest)


def block_scale(rng, dims, shards, least, largest):
    def one(position, shards_of):
        steps = jax.random.uniform(jax.random.fold_in(jax.random.fold_in(rng, 6), position), (shards_of,), jnp.float32, least / len(shards), largest / len(shards))
        return jnp.repeat(jnp.exp(steps), dims[position] // shards_of).reshape((-1,) + (1,) * (len(dims) - position - 1))

    loudness = one(*shards[0])
    for cut in shards[1:]:
        loudness = loudness * one(*cut)
    return loudness


def profile(number_of, total, most, lean):
    portions = [(1 << 20) // math.isqrt(standing ** lean) + 1 for standing in range(2, number_of + 1)]
    rest, holding = total - most - (number_of - 1), [1] * (number_of - 1)
    while rest > 0:
        free = [i for i in range(number_of - 1) if holding[i] < most]
        whole, budget = sum([portions[i] for i in free]), rest
        for i in free:
            extra = min(most - holding[i], max(1, budget * portions[i] // whole), rest)
            holding[i] = holding[i] + extra
            rest = rest - extra
    return np.array([most] + holding)


def ragged(rng, amount, total, limit, skew):
    if amount == 2:
        one = jax.random.randint(rng, (), max(1, total - limit), min(limit, total - 1) + 1)
        return jnp.stack([one, total - one])
    tallies = jnp.asarray(profile(amount, total, limit, skew), jnp.int32)
    pairs = (amount - 1) // 2
    giver, receiver = tallies[1:1 + 2 * pairs:2], tallies[2:2 + 2 * pairs:2]
    margin = jnp.minimum(giver - 1, limit - receiver)
    moved = jax.random.randint(jax.random.fold_in(rng, 1), (pairs,), 0, 1 << 20) % (margin + 1)
    tallies = tallies.at[1:1 + 2 * pairs:2].set(giver - moved).at[2:2 + 2 * pairs:2].set(receiver + moved)
    return tallies[jax.random.permutation(jax.random.fold_in(rng, 2), amount)]


def scatter_about(key, shape, scale, bound, cuts=(), held_as=jnp.bfloat16):
    level = block_scale(key, shape, cuts, -0.22, 0.18) if cuts else 1.0
    drawn = jax.random.normal(key, shape, jnp.float32) * scale * level
    return jnp.minimum(jnp.maximum(drawn, -bound), bound).astype(held_as)


def setup_inputs(seed: int = 0) -> dict:
    streams_of = jax.random.split(jax.random.key(seed), 9)
    return {
        "tokens": scatter_about(streams_of[0], (REQS * BLOCK, D), 1.0, 6.0, ((0, 64), (1, 8))),
        "norm_gain": jnp.clip(1.0 + 0.18 * jax.random.normal(streams_of[1], (D,), jnp.float32), 0.1, 1.9),
        "input_weight": scatter_about(streams_of[2], (D, 3, HEADS * HD), D ** -0.5, 0.125, ((2, 8),)),
        "output_weight": scatter_about(streams_of[3], (HEADS * HD, D), (HD // 4) ** -0.5, 1.0, ((0, 8),)),
        "cache_store": draw_cache_store(jax.random.fold_in(streams_of[8], 71), 0),
        "cache_length": ragged(streams_of[5], REQS, REQS * CMAX // 2, CMAX, 2).astype(jnp.int32),
        "placement": jax.random.permutation(streams_of[6], REQS).astype(jnp.int32),
        "accept": touch_ends((jax.random.randint(streams_of[7], (2, REQS * BLOCK), 0, 2) < 1).astype(jnp.int32), jax.random.fold_in(streams_of[7], 1), 0, 1),
    }


epsilon = 1e-05

def normalize(hidden, norm_gain):
    values = hidden.astype(jnp.float32)
    factor = lax.rsqrt(lax.optimization_barrier(jnp.mean(values * values, axis=-1, keepdims=True)) + epsilon)
    return (values * factor * norm_gain).astype(jnp.bfloat16)

def one_pass(hidden, norm_gain, input_weight, output_weight, cache_store, cache_length, placement, visible):
    total_width = HEADS * HD
    row_count = hidden.shape[0]
    projected = jnp.dot(normalize(hidden, norm_gain), input_weight.reshape(D, 3 * total_width), preferred_element_type=jnp.float32).astype(jnp.bfloat16)
    projected = projected.reshape(BLOCK, REQS, 3, HEADS, HD)
    visible_grid = visible.reshape(BLOCK, REQS)

    def per_request(request):
        queries = projected[:, request, 0].astype(jnp.float32)
        slot_index = placement[request]
        cache_pair = cache_store[slot_index]
        all_keys = jnp.concatenate([cache_pair[0].reshape(CMAX, HEADS, HD).astype(jnp.float32), projected[:, request, 1].astype(jnp.float32)], axis=0)
        all_values = jnp.concatenate([cache_pair[1].reshape(CMAX, HEADS, HD).astype(jnp.float32), projected[:, request, 2].astype(jnp.float32)], axis=0)
        live_keys = jnp.concatenate([jnp.arange(CMAX, dtype=jnp.int32) < cache_length[request], visible_grid[:, request] == 1], axis=0)
        scores = jnp.einsum('qhd,khd->hqk', queries, all_keys) / math.sqrt(HD)
        scores = jnp.where(live_keys[None, None, :], scores, jnp.float32(-1e+30))
        row_max = lax.optimization_barrier(jnp.max(scores, axis=2, keepdims=True))
        exponent = jnp.exp(scores - row_max)
        weights = (exponent / lax.optimization_barrier(jnp.sum(exponent, axis=2, keepdims=True))).astype(jnp.bfloat16)
        mixed = jnp.einsum('hqk,khd->qhd', weights.astype(jnp.float32), all_values)
        return mixed.reshape(BLOCK, total_width).astype(jnp.bfloat16)
    mixed = lax.map(per_request, jnp.arange(REQS, dtype=jnp.int32))
    mixed = jnp.transpose(mixed, (1, 0, 2)).reshape(row_count, total_width)
    branch = jnp.dot(mixed, output_weight, preferred_element_type=jnp.float32)
    return hidden.astype(jnp.float32) + branch

def reference(tokens, norm_gain, input_weight, output_weight, cache_store, cache_length, placement, accept):
    first_pass = one_pass(tokens.astype(jnp.float32), norm_gain, input_weight, output_weight, cache_store, cache_length, placement, accept[0])
    second = jnp.where(accept[0][:, None] == 1, first_pass, tokens.astype(jnp.float32))
    final = one_pass(second, norm_gain, input_weight, output_weight, cache_store, cache_length, placement, accept[1])
    return (first_pass, final)
```

```python
import math

import jax
import jax.numpy as jnp
from jax import lax
from jax.sharding import PartitionSpec as P

HD = 128
BLOCK = 256


epsilon = 1e-05


def slot_owner(placement):
    request_total = placement.shape[0]
    numbers = jnp.arange(request_total, dtype=jnp.int32)
    matches = placement[None, :] == numbers[:, None]
    return jnp.sum(jnp.where(matches, numbers[None, :], 0), axis=1)


def attend(queries, keys_new, values_new, cache_pair, length, visible):
    row_count = queries.shape[0]
    head_count = queries.shape[1] // HD
    cache_span = cache_pair.shape[1]
    query_heads = queries.reshape(row_count, head_count, HD)
    cache_keys = cache_pair[0].reshape(cache_span, head_count, HD)
    cache_values = cache_pair[1].reshape(cache_span, head_count, HD)
    cache_scores = jnp.einsum(
        "qhd,khd->hqk", query_heads, cache_keys, preferred_element_type=jnp.float32
    ) / math.sqrt(HD)
    inside = jnp.arange(cache_span, dtype=jnp.int32) < length
    cache_scores = jnp.where(inside[None, None, :], cache_scores, jnp.float32(-1e30))
    new_scores = jnp.einsum(
        "qhd,khd->hqk",
        query_heads,
        keys_new.reshape(row_count, head_count, HD),
        preferred_element_type=jnp.float32,
    ) / math.sqrt(HD)
    new_scores = jnp.where((visible == 1)[None, None, :], new_scores, jnp.float32(-1e30))
    scores = jnp.concatenate([cache_scores, new_scores], axis=2)
    row_max = jnp.max(scores, axis=2, keepdims=True)
    exponent = jnp.exp(scores - row_max)
    weights = (exponent / jnp.sum(exponent, axis=2, keepdims=True)).astype(jnp.bfloat16)
    mixed = jnp.einsum(
        "hqk,khd->qhd",
        weights[:, :, cache_span:],
        values_new.reshape(row_count, head_count, HD),
        preferred_element_type=jnp.float32,
    )
    mixed = mixed + jnp.einsum(
        "hqk,khd->qhd", weights[:, :, :cache_span], cache_values, preferred_element_type=jnp.float32
    )
    return mixed.reshape(row_count, head_count * HD).astype(jnp.bfloat16)


def on_device(
    tokens, norm_gain, input_weight, output_weight, cache_store, cache_length, placement, accept
):
    request_total = placement.shape[0]
    per_device = tokens.shape[0] // request_total
    local_width = tokens.shape[1]
    model_width = input_weight.shape[0]
    occupant = slot_owner(placement)
    device_index = lax.axis_index("req")
    feature_index = lax.axis_index("tp")
    my_request = occupant[device_index]
    my_length = cache_length[my_request]
    my_accept = accept.reshape(2, BLOCK, request_total)[:, :, my_request]
    my_gain = lax.dynamic_slice_in_dim(norm_gain, feature_index * local_width, local_width)
    flat_weight = input_weight.reshape(model_width, -1)
    column_weight = lax.all_to_all(output_weight, "tp", split_axis=1, concat_axis=0, tiled=True)

    by_slot = tokens.reshape(per_device, request_total, local_width)[:, occupant]
    held = lax.all_to_all(by_slot, "req", split_axis=1, concat_axis=0, tiled=True).reshape(
        BLOCK, local_width
    )
    hidden = held.astype(jnp.float32)

    def finish_pass(normed, visible):
        projected = jnp.dot(normed, flat_weight, preferred_element_type=jnp.float32).astype(
            jnp.bfloat16
        )
        queries, keys_new, values_new = jnp.split(projected, 3, axis=1)
        mixed = attend(queries, keys_new, values_new, cache_store[0], my_length, visible)
        mixed_all = lax.all_gather(mixed, "tp", axis=1, tiled=True)
        return jnp.dot(mixed_all, column_weight, preferred_element_type=jnp.float32)

    full = lax.all_gather(held, "tp", axis=1, tiled=True).astype(jnp.float32)
    factor = lax.rsqrt(jnp.mean(full * full, axis=-1, keepdims=True) + epsilon)
    normed = (full * factor * norm_gain).astype(jnp.bfloat16)
    first = hidden + finish_pass(normed, my_accept[0])

    second = jnp.where(my_accept[0][:, None] == 1, first, hidden)
    squares = lax.psum(jnp.sum(second * second, axis=-1, keepdims=True), "tp")
    factor = lax.rsqrt(squares / model_width + epsilon)
    normed_part = (second * factor * my_gain).astype(jnp.bfloat16)
    normed = lax.all_gather(normed_part, "tp", axis=1, tiled=True)
    final = second + finish_pass(normed, my_accept[1])

    def to_rows(values):
        back = lax.all_to_all(
            values.reshape(BLOCK, 1, local_width), "req", split_axis=0, concat_axis=1, tiled=True
        )
        return back[:, placement].reshape(per_device * request_total, local_width)

    return (to_rows(first), to_rows(final))


def solution(mesh):
    in_specs = (
        P("req", "tp"),
        P(),
        P(None, None, "tp"),
        P("tp", None),
        P("req", None, None, "tp"),
        P(),
        P(),
        P(),
    )
    out_specs = (P("req", "tp"), P("req", "tp"))
    return jax.shard_map(
        on_device, mesh=mesh, in_specs=in_specs, out_specs=out_specs, check_vma=False
    )
```

```python
import math

import jax
import jax.numpy as jnp
from jax import lax
from jax.sharding import PartitionSpec as P

HD = 128
BLOCK = 256


epsilon = 1e-05


def slot_owner(placement):
    request_total = placement.shape[0]
    numbers = jnp.arange(request_total, dtype=jnp.int32)
    matches = placement[None, :] == numbers[:, None]
    return jnp.sum(jnp.where(matches, numbers[None, :], 0), axis=1)


def attend(queries, keys_new, values_new, cache_pair, length, visible):
    row_count = queries.shape[0]
    head_count = queries.shape[1] // HD
    cache_span = cache_pair.shape[1]
    query_heads = queries.reshape(row_count, head_count, HD)
    cache_keys = cache_pair[0].reshape(cache_span, head_count, HD)
    cache_values = cache_pair[1].reshape(cache_span, head_count, HD)
    cache_scores = jnp.einsum(
        "qhd,khd->hqk", query_heads, cache_keys, preferred_element_type=jnp.float32
    ) / math.sqrt(HD)
    inside = jnp.arange(cache_span, dtype=jnp.int32) < length
    cache_scores = jnp.where(inside[None, None, :], cache_scores, jnp.float32(-1e30))
    new_scores = jnp.einsum(
        "qhd,khd->hqk",
        query_heads,
        keys_new.reshape(row_count, head_count, HD),
        preferred_element_type=jnp.float32,
    ) / math.sqrt(HD)
    new_scores = jnp.where((visible == 1)[None, None, :], new_scores, jnp.float32(-1e30))
    scores = jnp.concatenate([cache_scores, new_scores], axis=2)
    row_max = jnp.max(scores, axis=2, keepdims=True)
    exponent = jnp.exp(scores - row_max)
    weights = (exponent / jnp.sum(exponent, axis=2, keepdims=True)).astype(jnp.bfloat16)
    mixed = jnp.einsum(
        "hqk,khd->qhd",
        weights[:, :, cache_span:],
        values_new.reshape(row_count, head_count, HD),
        preferred_element_type=jnp.float32,
    )
    mixed = mixed + jnp.einsum(
        "hqk,khd->qhd", weights[:, :, :cache_span], cache_values, preferred_element_type=jnp.float32
    )
    return mixed.reshape(row_count, head_count * HD).astype(jnp.bfloat16)


def on_device(
    tokens, norm_gain, input_weight, output_weight, cache_store, cache_length, placement, accept
):
    request_total = placement.shape[0]
    per_device = tokens.shape[0] // request_total
    local_width = tokens.shape[1]
    model_width = input_weight.shape[0]
    occupant = slot_owner(placement)
    device_index = lax.axis_index("req")
    feature_index = lax.axis_index("tp")
    my_request = occupant[device_index]
    my_length = cache_length[my_request]
    my_accept = accept.reshape(2, BLOCK, request_total)[:, :, my_request]
    flat_weight = input_weight.reshape(model_width, -1)

    by_slot = tokens.reshape(per_device, request_total, local_width)[:, occupant]
    held = lax.all_to_all(by_slot, "req", split_axis=1, concat_axis=0, tiled=True).reshape(
        BLOCK, local_width
    )

    def partial_branch(hidden, visible):
        factor = lax.rsqrt(jnp.mean(hidden * hidden, axis=-1, keepdims=True) + epsilon)
        normed = (hidden * factor * norm_gain).astype(jnp.bfloat16)
        projected = jnp.dot(normed, flat_weight, preferred_element_type=jnp.float32).astype(
            jnp.bfloat16
        )
        queries, keys_new, values_new = jnp.split(projected, 3, axis=1)
        mixed = attend(queries, keys_new, values_new, cache_store[0], my_length, visible)
        return jnp.dot(mixed, output_weight, preferred_element_type=jnp.float32)

    full = lax.all_gather(held, "tp", axis=1, tiled=True).astype(jnp.float32)
    first_full = full + lax.psum(partial_branch(full, my_accept[0]), "tp")
    second_full = jnp.where(my_accept[0][:, None] == 1, first_full, full)
    branch = lax.psum_scatter(
        partial_branch(second_full, my_accept[1]), "tp", scatter_dimension=1, tiled=True
    )
    mine = lambda values: lax.dynamic_slice_in_dim(values, feature_index * local_width, local_width, axis=1)
    first = mine(first_full)
    final = mine(second_full) + branch

    def to_rows(values):
        back = lax.all_to_all(
            values.reshape(BLOCK, 1, local_width), "req", split_axis=0, concat_axis=1, tiled=True
        )
        return back[:, placement].reshape(per_device * request_total, local_width)

    return (to_rows(first), to_rows(final))


def solution(mesh):
    in_specs = (
        P("req", "tp"),
        P(),
        P(None, None, "tp"),
        P("tp", None),
        P("req", None, None, "tp"),
        P(),
        P(),
        P(),
    )
    out_specs = (P("req", "tp"), P("req", "tp"))
    return jax.shard_map(
        on_device, mesh=mesh, in_specs=in_specs, out_specs=out_specs, check_vma=False
    )
```

```python
import math

import jax
import jax.numpy as jnp
from jax import lax
from jax.sharding import PartitionSpec as P

HD = 128
BLOCK = 256


epsilon = 1e-05


def slot_owner(placement):
    request_total = placement.shape[0]
    numbers = jnp.arange(request_total, dtype=jnp.int32)
    matches = placement[None, :] == numbers[:, None]
    return jnp.sum(jnp.where(matches, numbers[None, :], 0), axis=1)


def attend(queries, keys_new, values_new, cache_pair, length, visible):
    row_count = queries.shape[0]
    head_count = queries.shape[1] // HD
    cache_span = cache_pair.shape[1]
    query_heads = queries.reshape(row_count, head_count, HD)
    cache_keys = cache_pair[0].reshape(cache_span, head_count, HD)
    cache_values = cache_pair[1].reshape(cache_span, head_count, HD)
    cache_scores = jnp.einsum(
        "qhd,khd->hqk", query_heads, cache_keys, preferred_element_type=jnp.float32
    ) / math.sqrt(HD)
    inside = jnp.arange(cache_span, dtype=jnp.int32) < length
    cache_scores = jnp.where(inside[None, None, :], cache_scores, jnp.float32(-1e30))
    new_scores = jnp.einsum(
        "qhd,khd->hqk",
        query_heads,
        keys_new.reshape(row_count, head_count, HD),
        preferred_element_type=jnp.float32,
    ) / math.sqrt(HD)
    new_scores = jnp.where((visible == 1)[None, None, :], new_scores, jnp.float32(-1e30))
    scores = jnp.concatenate([cache_scores, new_scores], axis=2)
    row_max = jnp.max(scores, axis=2, keepdims=True)
    exponent = jnp.exp(scores - row_max)
    weights = (exponent / jnp.sum(exponent, axis=2, keepdims=True)).astype(jnp.bfloat16)
    mixed = jnp.einsum(
        "hqk,khd->qhd",
        weights[:, :, cache_span:],
        values_new.reshape(row_count, head_count, HD),
        preferred_element_type=jnp.float32,
    )
    mixed = mixed + jnp.einsum(
        "hqk,khd->qhd", weights[:, :, :cache_span], cache_values, preferred_element_type=jnp.float32
    )
    return mixed.reshape(row_count, head_count * HD).astype(jnp.bfloat16)


def gather_tp(blocks):
    return lax.all_to_all(blocks, "tp", split_axis=0, concat_axis=0, tiled=True)


def spread(value, count):
    return jnp.broadcast_to(value[None], (count,) + value.shape)


def side_by_side(blocks):
    count, rows, width = blocks.shape
    return jnp.transpose(blocks, (1, 0, 2)).reshape(rows, count * width)


def on_device(
    tokens, norm_gain, input_weight, output_weight, cache_store, cache_length, placement, accept
):
    request_total = placement.shape[0]
    per_device = tokens.shape[0] // request_total
    local_width = tokens.shape[1]
    model_width = input_weight.shape[0]
    tp_count = model_width // local_width
    head_width = output_weight.shape[0]
    occupant = slot_owner(placement)
    device_index = lax.axis_index("req")
    my_request = occupant[device_index]
    my_length = cache_length[my_request]
    my_accept = accept.reshape(2, BLOCK, request_total)[:, :, my_request]
    flat_weight = input_weight.reshape(model_width, -1)

    by_slot = tokens.reshape(per_device, request_total, local_width)[:, occupant]
    held = lax.all_to_all(by_slot, "req", split_axis=1, concat_axis=0, tiled=True).reshape(
        BLOCK, local_width
    )
    hidden = held.astype(jnp.float32)

    weight_blocks = jnp.transpose(
        output_weight.reshape(head_width, tp_count, local_width), (1, 0, 2)
    )
    arrived = gather_tp(jnp.concatenate([spread(held, tp_count), weight_blocks], axis=2))
    full = side_by_side(arrived[:, :, :local_width]).astype(jnp.float32)
    column_weight = arrived[:, :, local_width:].reshape(tp_count * head_width, local_width)

    def branch_of(full_hidden, visible):
        factor = lax.rsqrt(jnp.mean(full_hidden * full_hidden, axis=-1, keepdims=True) + epsilon)
        normed = (full_hidden * factor * norm_gain).astype(jnp.bfloat16)
        projected = jnp.dot(normed, flat_weight, preferred_element_type=jnp.float32).astype(
            jnp.bfloat16
        )
        queries, keys_new, values_new = jnp.split(projected, 3, axis=1)
        mixed = attend(queries, keys_new, values_new, cache_store[0], my_length, visible)
        mixed_all = side_by_side(gather_tp(spread(mixed, tp_count)))
        return jnp.dot(mixed_all, column_weight, preferred_element_type=jnp.float32)

    first = hidden + branch_of(full, my_accept[0])
    second = jnp.where(my_accept[0][:, None] == 1, first, hidden)
    second_full = side_by_side(gather_tp(spread(second, tp_count)))
    final = second + branch_of(second_full, my_accept[1])

    both = jnp.concatenate([first, final], axis=1).reshape(BLOCK, 1, 2 * local_width)
    back = lax.all_to_all(both, "req", split_axis=0, concat_axis=1, tiled=True)[:, placement]
    back = back.reshape(per_device * request_total, 2 * local_width)
    return (back[:, :local_width], back[:, local_width:])


def solution(mesh):
    in_specs = (
        P("req", "tp"),
        P(),
        P(None, None, "tp"),
        P("tp", None),
        P("req", None, None, "tp"),
        P(),
        P(),
        P(),
    )
    out_specs = (P("req", "tp"), P("req", "tp"))
    return jax.shard_map(
        on_device, mesh=mesh, in_specs=in_specs, out_specs=out_specs, check_vma=False
    )
```

```python
import math

import jax
import jax.numpy as jnp
from jax import lax
from jax.sharding import PartitionSpec as P

HD = 128
BLOCK = 256


epsilon = 1e-05


def slot_owner(placement):
    request_total = placement.shape[0]
    numbers = jnp.arange(request_total, dtype=jnp.int32)
    matches = placement[None, :] == numbers[:, None]
    return jnp.sum(jnp.where(matches, numbers[None, :], 0), axis=1)


def attend(queries, keys_new, values_new, cache_pair, length, visible):
    row_count = queries.shape[0]
    head_count = queries.shape[1] // HD
    cache_span = cache_pair.shape[1]
    query_heads = queries.reshape(row_count, head_count, HD)
    cache_keys = cache_pair[0].reshape(cache_span, head_count, HD)
    cache_values = cache_pair[1].reshape(cache_span, head_count, HD)
    cache_scores = jnp.einsum(
        "qhd,khd->hqk", query_heads, cache_keys, preferred_element_type=jnp.float32
    ) / math.sqrt(HD)
    inside = jnp.arange(cache_span, dtype=jnp.int32) < length
    cache_scores = jnp.where(inside[None, None, :], cache_scores, jnp.float32(-1e30))
    new_scores = jnp.einsum(
        "qhd,khd->hqk",
        query_heads,
        keys_new.reshape(row_count, head_count, HD),
        preferred_element_type=jnp.float32,
    ) / math.sqrt(HD)
    new_scores = jnp.where((visible == 1)[None, None, :], new_scores, jnp.float32(-1e30))
    scores = jnp.concatenate([cache_scores, new_scores], axis=2)
    row_max = jnp.max(scores, axis=2, keepdims=True)
    exponent = jnp.exp(scores - row_max)
    weights = (exponent / jnp.sum(exponent, axis=2, keepdims=True)).astype(jnp.bfloat16)
    mixed = jnp.einsum(
        "hqk,khd->qhd",
        weights[:, :, cache_span:],
        values_new.reshape(row_count, head_count, HD),
        preferred_element_type=jnp.float32,
    )
    mixed = mixed + jnp.einsum(
        "hqk,khd->qhd", weights[:, :, :cache_span], cache_values, preferred_element_type=jnp.float32
    )
    return mixed.reshape(row_count, head_count * HD).astype(jnp.bfloat16)


def gather_tp(blocks):
    return lax.all_to_all(blocks, "tp", split_axis=0, concat_axis=0, tiled=True)


def spread(value, count):
    return jnp.broadcast_to(value[None], (count,) + value.shape)


def side_by_side(blocks):
    count, rows, width = blocks.shape
    return jnp.transpose(blocks, (1, 0, 2)).reshape(rows, count * width)


def on_device(
    tokens, norm_gain, input_weight, output_weight, cache_store, cache_length, placement, accept
):
    request_total = placement.shape[0]
    per_device = tokens.shape[0] // request_total
    local_width = tokens.shape[1]
    model_width = input_weight.shape[0]
    tp_count = model_width // local_width
    head_width = output_weight.shape[0]
    occupant = slot_owner(placement)
    device_index = lax.axis_index("req")
    my_request = occupant[device_index]
    my_length = cache_length[my_request]
    my_accept = accept.reshape(2, BLOCK, request_total)[:, :, my_request]
    flat_weight = input_weight.reshape(model_width, -1)

    by_slot = tokens.reshape(per_device, request_total, local_width)[:, occupant]
    held = lax.all_to_all(by_slot, "req", split_axis=1, concat_axis=0, tiled=True).reshape(
        BLOCK, local_width
    )
    hidden = held.astype(jnp.float32)

    tp_index = lax.axis_index("tp")
    weight_blocks = jnp.transpose(
        output_weight.reshape(head_width, tp_count, local_width), (1, 0, 2)
    )
    received = [lax.dynamic_index_in_dim(weight_blocks, tp_index, keepdims=False)]
    for shift in range(1, tp_count):
        outgoing = lax.dynamic_index_in_dim(weight_blocks, (tp_index + shift) % tp_count, keepdims=False)
        pairs = [(k, (k + shift) % tp_count) for k in range(tp_count)]
        received.append(lax.ppermute(outgoing, "tp", pairs))
    sources = (tp_index - jnp.arange(tp_count)) % tp_count
    ordered = jnp.zeros((tp_count, head_width, local_width), output_weight.dtype)
    ordered = ordered.at[sources].set(jnp.stack(received))
    column_weight = ordered.reshape(tp_count * head_width, local_width)
    full = side_by_side(gather_tp(spread(held, tp_count))).astype(jnp.float32)

    def branch_of(normed, visible):
        projected = jnp.dot(normed, flat_weight, preferred_element_type=jnp.float32).astype(
            jnp.bfloat16
        )
        queries, keys_new, values_new = jnp.split(projected, 3, axis=1)
        mixed = attend(queries, keys_new, values_new, cache_store[0], my_length, visible)
        mixed_all = side_by_side(gather_tp(spread(mixed, tp_count)))
        return jnp.dot(mixed_all, column_weight, preferred_element_type=jnp.float32)

    factor = lax.rsqrt(jnp.mean(full * full, axis=-1, keepdims=True) + epsilon)
    normed = (full * factor * norm_gain).astype(jnp.bfloat16)
    first = hidden + branch_of(normed, my_accept[0])
    second = jnp.where(my_accept[0][:, None] == 1, first, hidden)
    partial = jnp.sum(second * second, axis=-1)
    squares = jnp.sum(gather_tp(spread(partial, tp_count)), axis=0)[:, None]
    factor = lax.rsqrt(squares / model_width + epsilon)
    my_gain = lax.dynamic_slice_in_dim(norm_gain, tp_index * local_width, local_width)
    normed_part = (second * factor * my_gain).astype(jnp.bfloat16)
    normed = side_by_side(gather_tp(spread(normed_part, tp_count)))
    final = second + branch_of(normed, my_accept[1])

    both = jnp.concatenate([first, final], axis=1).reshape(BLOCK, 1, 2 * local_width)
    back = lax.all_to_all(both, "req", split_axis=0, concat_axis=1, tiled=True)[:, placement]
    back = back.reshape(per_device * request_total, 2 * local_width)
    return (back[:, :local_width], back[:, local_width:])


def solution(mesh):
    in_specs = (
        P("req", "tp"),
        P(),
        P(None, None, "tp"),
        P("tp", None),
        P("req", None, None, "tp"),
        P(),
        P(),
        P(),
    )
    out_specs = (P("req", "tp"), P("req", "tp"))
    return jax.shard_map(
        on_device, mesh=mesh, in_specs=in_specs, out_specs=out_specs, check_vma=False
    )
```

```python
import math

import jax
import jax.numpy as jnp
from jax import lax
from jax.sharding import PartitionSpec as P

HD = 128
BLOCK = 256


epsilon = 1e-05


def slot_owner(placement):
    request_total = placement.shape[0]
    numbers = jnp.arange(request_total, dtype=jnp.int32)
    matches = placement[None, :] == numbers[:, None]
    return jnp.sum(jnp.where(matches, numbers[None, :], 0), axis=1)


def attend(queries, keys_new, values_new, cache_pair, length, visible):
    row_count = queries.shape[0]
    head_count = queries.shape[1] // HD
    cache_span = cache_pair.shape[1]
    query_heads = queries.reshape(row_count, head_count, HD)
    cache_keys = cache_pair[0].reshape(cache_span, head_count, HD)
    cache_values = cache_pair[1].reshape(cache_span, head_count, HD)
    cache_scores = jnp.einsum(
        "qhd,khd->hqk", query_heads, cache_keys, preferred_element_type=jnp.float32
    ) / math.sqrt(HD)
    inside = jnp.arange(cache_span, dtype=jnp.int32) < length
    cache_scores = jnp.where(inside[None, None, :], cache_scores, jnp.float32(-1e30))
    new_scores = jnp.einsum(
        "qhd,khd->hqk",
        query_heads,
        keys_new.reshape(row_count, head_count, HD),
        preferred_element_type=jnp.float32,
    ) / math.sqrt(HD)
    new_scores = jnp.where((visible == 1)[None, None, :], new_scores, jnp.float32(-1e30))
    scores = jnp.concatenate([cache_scores, new_scores], axis=2)
    row_max = jnp.max(scores, axis=2, keepdims=True)
    exponent = jnp.exp(scores - row_max)
    weights = (exponent / jnp.sum(exponent, axis=2, keepdims=True)).astype(jnp.bfloat16)
    mixed = jnp.einsum(
        "hqk,khd->qhd",
        weights[:, :, cache_span:],
        values_new.reshape(row_count, head_count, HD),
        preferred_element_type=jnp.float32,
    )
    mixed = mixed + jnp.einsum(
        "hqk,khd->qhd", weights[:, :, :cache_span], cache_values, preferred_element_type=jnp.float32
    )
    return mixed.reshape(row_count, head_count * HD).astype(jnp.bfloat16)


def gather_tp(blocks):
    return lax.all_to_all(blocks, "tp", split_axis=0, concat_axis=0, tiled=True)


def spread(value, count):
    return jnp.broadcast_to(value[None], (count,) + value.shape)


def side_by_side(blocks):
    count, rows, width = blocks.shape
    return jnp.transpose(blocks, (1, 0, 2)).reshape(rows, count * width)


def on_device(
    tokens, norm_gain, input_weight, output_weight, cache_store, cache_length, placement, accept
):
    request_total = placement.shape[0]
    per_device = tokens.shape[0] // request_total
    local_width = tokens.shape[1]
    model_width = input_weight.shape[0]
    tp_count = model_width // local_width
    head_width = output_weight.shape[0]
    occupant = slot_owner(placement)
    device_index = lax.axis_index("req")
    my_request = occupant[device_index]
    my_length = cache_length[my_request]
    my_accept = accept.reshape(2, BLOCK, request_total)[:, :, my_request]
    flat_weight = input_weight.reshape(model_width, -1)

    by_slot = tokens.reshape(per_device, request_total, local_width)[:, occupant]
    held = lax.all_to_all(by_slot, "req", split_axis=1, concat_axis=0, tiled=True).reshape(
        BLOCK, local_width
    )
    hidden = held.astype(jnp.float32)

    tp_index = lax.axis_index("tp")
    weight_blocks = jnp.transpose(
        output_weight.reshape(head_width, tp_count, local_width), (1, 0, 2)
    )
    arrived = gather_tp(jnp.concatenate([spread(held, tp_count), weight_blocks], axis=2))
    full = side_by_side(arrived[:, :, :local_width]).astype(jnp.float32)
    column_weight = arrived[:, :, local_width:].reshape(tp_count * head_width, local_width)

    def branch_of(normed, visible):
        projected = jnp.dot(normed, flat_weight, preferred_element_type=jnp.float32).astype(
            jnp.bfloat16
        )
        queries, keys_new, values_new = jnp.split(projected, 3, axis=1)
        mixed = attend(queries, keys_new, values_new, cache_store[0], my_length, visible)
        mixed_all = side_by_side(gather_tp(spread(mixed, tp_count)))
        return jnp.dot(mixed_all, column_weight, preferred_element_type=jnp.float32)

    factor = lax.rsqrt(jnp.mean(full * full, axis=-1, keepdims=True) + epsilon)
    normed = (full * factor * norm_gain).astype(jnp.bfloat16)
    first = hidden + branch_of(normed, my_accept[0])
    second = jnp.where(my_accept[0][:, None] == 1, first, hidden)
    partial = jnp.sum(second * second, axis=-1)
    squares = jnp.sum(gather_tp(spread(partial, tp_count)), axis=0)[:, None]
    factor = lax.rsqrt(squares / model_width + epsilon)
    my_gain = lax.dynamic_slice_in_dim(norm_gain, tp_index * local_width, local_width)
    normed_part = (second * factor * my_gain).astype(jnp.bfloat16)
    normed = side_by_side(gather_tp(spread(normed_part, tp_count)))
    final = second + branch_of(normed, my_accept[1])

    both = jnp.concatenate([first, final], axis=1).reshape(BLOCK, 1, 2 * local_width)
    back = lax.all_to_all(both, "req", split_axis=0, concat_axis=1, tiled=True)[:, placement]
    back = back.reshape(per_device * request_total, 2 * local_width)
    return (back[:, :local_width], back[:, local_width:])


def solution(mesh):
    in_specs = (
        P("req", "tp"),
        P(),
        P(None, None, "tp"),
        P("tp", None),
        P("req", None, None, "tp"),
        P(),
        P(),
        P(),
    )
    out_specs = (P("req", "tp"), P("req", "tp"))
    return jax.shard_map(
        on_device, mesh=mesh, in_specs=in_specs, out_specs=out_specs, check_vma=False
    )
```

```python
import math

import jax
import jax.numpy as jnp
from jax import lax
from jax.sharding import Mesh, PartitionSpec as P

HD = 128
BLOCK = 256


epsilon = 1e-05


def slot_owner(placement):
    request_total = placement.shape[0]
    numbers = jnp.arange(request_total, dtype=jnp.int32)
    matches = placement[None, :] == numbers[:, None]
    return jnp.sum(jnp.where(matches, numbers[None, :], 0), axis=1)


def attend(queries, keys_new, values_new, cache_pair, length, visible):
    row_count = queries.shape[0]
    head_count = queries.shape[1] // HD
    cache_span = cache_pair.shape[1]
    query_heads = queries.reshape(row_count, head_count, HD)
    cache_keys = cache_pair[0].reshape(cache_span, head_count, HD)
    cache_values = cache_pair[1].reshape(cache_span, head_count, HD)
    cache_scores = jnp.einsum(
        "qhd,khd->hqk", query_heads, cache_keys, preferred_element_type=jnp.float32
    ) / math.sqrt(HD)
    inside = jnp.arange(cache_span, dtype=jnp.int32) < length
    cache_scores = jnp.where(inside[None, None, :], cache_scores, jnp.float32(-1e30))
    new_scores = jnp.einsum(
        "qhd,khd->hqk",
        query_heads,
        keys_new.reshape(row_count, head_count, HD),
        preferred_element_type=jnp.float32,
    ) / math.sqrt(HD)
    new_scores = jnp.where((visible == 1)[None, None, :], new_scores, jnp.float32(-1e30))
    scores = jnp.concatenate([cache_scores, new_scores], axis=2)
    row_max = jnp.max(scores, axis=2, keepdims=True)
    exponent = jnp.exp(scores - row_max)
    weights = (exponent / jnp.sum(exponent, axis=2, keepdims=True)).astype(jnp.bfloat16)
    mixed = jnp.einsum(
        "hqk,khd->qhd",
        weights[:, :, cache_span:],
        values_new.reshape(row_count, head_count, HD),
        preferred_element_type=jnp.float32,
    )
    mixed = mixed + jnp.einsum(
        "hqk,khd->qhd", weights[:, :, :cache_span], cache_values, preferred_element_type=jnp.float32
    )
    return mixed.reshape(row_count, head_count * HD).astype(jnp.bfloat16)


TP = ("x", "c")


def gather_tp(blocks):
    return lax.all_to_all(blocks, TP, split_axis=0, concat_axis=0, tiled=True)


def gather_two_stage(value):
    across = lax.all_to_all(
        spread(value, lax.axis_size("x")), "x", split_axis=0, concat_axis=0, tiled=True
    )
    both = lax.all_to_all(
        spread(across, lax.axis_size("c")), "c", split_axis=0, concat_axis=0, tiled=True
    )
    both = jnp.swapaxes(both, 0, 1)
    return both.reshape((-1,) + value.shape)


def spread(value, count):
    return jnp.broadcast_to(value[None], (count,) + value.shape)


def side_by_side(blocks):
    count, rows, width = blocks.shape
    return jnp.transpose(blocks, (1, 0, 2)).reshape(rows, count * width)


def on_device(
    tokens, norm_gain, input_weight, output_weight, cache_store, cache_length, placement, accept
):
    request_total = placement.shape[0]
    per_device = tokens.shape[0] // request_total
    local_width = tokens.shape[1]
    model_width = input_weight.shape[0]
    tp_count = model_width // local_width
    head_width = output_weight.shape[0]
    occupant = slot_owner(placement)
    device_index = lax.axis_index("req")
    my_request = occupant[device_index]
    my_length = cache_length[my_request]
    my_accept = accept.reshape(2, BLOCK, request_total)[:, :, my_request]
    flat_weight = input_weight.reshape(model_width, -1)

    by_slot = tokens.reshape(per_device, request_total, local_width)[:, occupant]
    held = lax.all_to_all(by_slot, "req", split_axis=1, concat_axis=0, tiled=True).reshape(
        BLOCK, local_width
    )
    hidden = held.astype(jnp.float32)

    tp_index = lax.axis_index(TP)
    weight_blocks = jnp.transpose(
        output_weight.reshape(head_width, tp_count, local_width), (1, 0, 2)
    )
    arrived = gather_tp(jnp.concatenate([spread(held, tp_count), weight_blocks], axis=2))
    full = side_by_side(arrived[:, :, :local_width]).astype(jnp.float32)
    column_weight = arrived[:, :, local_width:].reshape(tp_count * head_width, local_width)

    def branch_of(normed, visible):
        projected = jnp.dot(normed, flat_weight, preferred_element_type=jnp.float32).astype(
            jnp.bfloat16
        )
        queries, keys_new, values_new = jnp.split(projected, 3, axis=1)
        mixed = attend(queries, keys_new, values_new, cache_store[0], my_length, visible)
        mixed_all = side_by_side(gather_two_stage(mixed))
        return jnp.dot(mixed_all, column_weight, preferred_element_type=jnp.float32)

    factor = lax.rsqrt(jnp.mean(full * full, axis=-1, keepdims=True) + epsilon)
    normed = (full * factor * norm_gain).astype(jnp.bfloat16)
    first = hidden + branch_of(normed, my_accept[0])
    second = jnp.where(my_accept[0][:, None] == 1, first, hidden)
    partial = jnp.sum(second * second, axis=-1)
    squares = jnp.sum(gather_tp(spread(partial, tp_count)), axis=0)[:, None]
    factor = lax.rsqrt(squares / model_width + epsilon)
    my_gain = lax.dynamic_slice_in_dim(norm_gain, tp_index * local_width, local_width)
    normed_part = (second * factor * my_gain).astype(jnp.bfloat16)
    normed = side_by_side(gather_two_stage(normed_part))
    final = second + branch_of(normed, my_accept[1])

    both = jnp.concatenate([first, final], axis=1).reshape(BLOCK, 1, 2 * local_width)
    back = lax.all_to_all(both, "req", split_axis=0, concat_axis=1, tiled=True)[:, placement]
    back = back.reshape(per_device * request_total, 2 * local_width)
    return (back[:, :local_width], back[:, local_width:])


def solution(mesh):
    tp_size = mesh.shape["tp"]
    mesh = Mesh(
        mesh.devices.reshape(mesh.shape["req"], tp_size // 2, 2), ("req", "x", "c")
    )
    in_specs = (
        P("req", TP),
        P(),
        P(None, None, TP),
        P(TP, None),
        P("req", None, None, TP),
        P(),
        P(),
        P(),
    )
    out_specs = (P("req", TP), P("req", TP))
    return jax.shard_map(
        on_device, mesh=mesh, in_specs=in_specs, out_specs=out_specs, check_vma=False
    )
```

```python
import math

import jax
import jax.numpy as jnp
from jax import lax
from jax.sharding import Mesh, PartitionSpec as P

HD = 128
BLOCK = 256


epsilon = 1e-05


def slot_owner(placement):
    request_total = placement.shape[0]
    numbers = jnp.arange(request_total, dtype=jnp.int32)
    matches = placement[None, :] == numbers[:, None]
    return jnp.sum(jnp.where(matches, numbers[None, :], 0), axis=1)


def attend(queries, keys_new, values_new, cache_pair, length, visible):
    row_count = queries.shape[0]
    head_count = queries.shape[1] // HD
    cache_span = cache_pair.shape[1]
    query_heads = queries.reshape(row_count, head_count, HD)
    cache_keys = cache_pair[0].reshape(cache_span, head_count, HD)
    cache_values = cache_pair[1].reshape(cache_span, head_count, HD)
    cache_scores = jnp.einsum(
        "qhd,khd->hqk", query_heads, cache_keys, preferred_element_type=jnp.float32
    ) / math.sqrt(HD)
    inside = jnp.arange(cache_span, dtype=jnp.int32) < length
    cache_scores = jnp.where(inside[None, None, :], cache_scores, jnp.float32(-1e30))
    new_scores = jnp.einsum(
        "qhd,khd->hqk",
        query_heads,
        keys_new.reshape(row_count, head_count, HD),
        preferred_element_type=jnp.float32,
    ) / math.sqrt(HD)
    new_scores = jnp.where((visible == 1)[None, None, :], new_scores, jnp.float32(-1e30))
    scores = jnp.concatenate([cache_scores, new_scores], axis=2)
    row_max = jnp.max(scores, axis=2, keepdims=True)
    exponent = jnp.exp(scores - row_max)
    weights = (exponent / jnp.sum(exponent, axis=2, keepdims=True)).astype(jnp.bfloat16)
    mixed = jnp.einsum(
        "hqk,khd->qhd",
        weights[:, :, cache_span:],
        values_new.reshape(row_count, head_count, HD),
        preferred_element_type=jnp.float32,
    )
    mixed = mixed + jnp.einsum(
        "hqk,khd->qhd", weights[:, :, :cache_span], cache_values, preferred_element_type=jnp.float32
    )
    return mixed.reshape(row_count, head_count * HD).astype(jnp.bfloat16)


TP = ("x", "c")


def gather_tp(blocks):
    return lax.all_to_all(blocks, TP, split_axis=0, concat_axis=0, tiled=True)


def gather_two_stage(value):
    across = lax.all_to_all(
        spread(value, lax.axis_size("x")), "x", split_axis=0, concat_axis=0, tiled=True
    )
    both = lax.all_to_all(
        spread(across, lax.axis_size("c")), "c", split_axis=0, concat_axis=0, tiled=True
    )
    both = jnp.swapaxes(both, 0, 1)
    return both.reshape((-1,) + value.shape)


def spread(value, count):
    return jnp.broadcast_to(value[None], (count,) + value.shape)


def side_by_side(blocks):
    count, rows, width = blocks.shape
    return jnp.transpose(blocks, (1, 0, 2)).reshape(rows, count * width)


def on_device(
    tokens, norm_gain, input_weight, output_weight, cache_store, cache_length, placement, accept
):
    request_total = placement.shape[0]
    per_device = tokens.shape[0] // request_total
    local_width = tokens.shape[1]
    model_width = input_weight.shape[0]
    tp_count = model_width // local_width
    head_width = output_weight.shape[0]
    occupant = slot_owner(placement)
    device_index = lax.axis_index("req")
    my_request = occupant[device_index]
    my_length = cache_length[my_request]
    my_accept = accept.reshape(2, BLOCK, request_total)[:, :, my_request]
    block_weight = input_weight.reshape(tp_count, local_width, -1)
    numbers = jnp.arange(request_total, dtype=jnp.int32)
    slot_pick = (placement[:, None] == numbers[None, :]).astype(tokens.dtype)

    by_slot = jnp.einsum(
        "jrf,rs->jsf",
        tokens.reshape(per_device, request_total, local_width),
        slot_pick,
        preferred_element_type=jnp.float32,
    ).astype(tokens.dtype)
    held = lax.all_to_all(by_slot, "req", split_axis=1, concat_axis=0, tiled=True).reshape(
        BLOCK, local_width
    )
    hidden = held.astype(jnp.float32)

    tp_index = lax.axis_index(TP)
    weight_blocks = jnp.transpose(
        output_weight.reshape(head_width, tp_count, local_width), (1, 0, 2)
    )
    arrived = gather_tp(jnp.concatenate([spread(held, tp_count), weight_blocks], axis=2))
    full = arrived[:, :, :local_width].astype(jnp.float32)
    column_weight = arrived[:, :, local_width:]
    gain_blocks = norm_gain.reshape(tp_count, 1, local_width)

    def branch_of(normed, visible):
        projected = jnp.einsum(
            "kpf,kfo->po", normed, block_weight, preferred_element_type=jnp.float32
        ).astype(jnp.bfloat16)
        queries, keys_new, values_new = jnp.split(projected, 3, axis=1)
        mixed = attend(queries, keys_new, values_new, cache_store[0], my_length, visible)
        return jnp.einsum(
            "kph,khf->pf", gather_two_stage(mixed), column_weight, preferred_element_type=jnp.float32
        )

    squares = jnp.sum(full * full, axis=(0, 2))[None, :, None]
    factor = lax.rsqrt(squares / model_width + epsilon)
    normed = (full * factor * gain_blocks).astype(jnp.bfloat16)
    first = hidden + branch_of(normed, my_accept[0])
    second = jnp.where(my_accept[0][:, None] == 1, first, hidden)
    partial = jnp.sum(second * second, axis=-1)
    squares = jnp.sum(gather_tp(spread(partial, tp_count)), axis=0)[:, None]
    factor = lax.rsqrt(squares / model_width + epsilon)
    my_gain = lax.dynamic_slice_in_dim(norm_gain, tp_index * local_width, local_width)
    normed_part = (second * factor * my_gain).astype(jnp.bfloat16)
    normed = gather_two_stage(normed_part)
    final = second + branch_of(normed, my_accept[1])

    both = jnp.concatenate([first, final], axis=1).reshape(BLOCK, 1, 2 * local_width)
    back = lax.all_to_all(both, "req", split_axis=0, concat_axis=1, tiled=True)[:, placement]
    back = back.reshape(per_device * request_total, 2 * local_width)
    return (back[:, :local_width], back[:, local_width:])


def solution(mesh):
    tp_size = mesh.shape["tp"]
    mesh = Mesh(
        mesh.devices.reshape(mesh.shape["req"], tp_size // 2, 2), ("req", "x", "c")
    )
    in_specs = (
        P("req", TP),
        P(),
        P(None, None, TP),
        P(TP, None),
        P("req", None, None, TP),
        P(),
        P(),
        P(),
    )
    out_specs = (P("req", TP), P("req", TP))
    return jax.shard_map(
        on_device, mesh=mesh, in_specs=in_specs, out_specs=out_specs, check_vma=False
    )
```

```python
import math

import jax
import jax.numpy as jnp
from jax import lax
from jax.sharding import Mesh, PartitionSpec as P

HD = 128
BLOCK = 256


epsilon = 1e-05


def slot_owner(placement):
    request_total = placement.shape[0]
    numbers = jnp.arange(request_total, dtype=jnp.int32)
    matches = placement[None, :] == numbers[:, None]
    return jnp.sum(jnp.where(matches, numbers[None, :], 0), axis=1)


def attend(queries, keys_new, values_new, cache_pair, length, visible):
    row_count = queries.shape[0]
    head_count = queries.shape[1] // HD
    cache_span = cache_pair.shape[1]
    query_heads = queries.reshape(row_count, head_count, HD)
    cache_keys = cache_pair[0].reshape(cache_span, head_count, HD)
    cache_values = cache_pair[1].reshape(cache_span, head_count, HD)
    cache_scores = jnp.einsum(
        "qhd,khd->hqk", query_heads, cache_keys, preferred_element_type=jnp.float32
    ) / math.sqrt(HD)
    inside = jnp.arange(cache_span, dtype=jnp.int32) < length
    cache_scores = jnp.where(inside[None, None, :], cache_scores, jnp.float32(-1e30))
    new_scores = jnp.einsum(
        "qhd,khd->hqk",
        query_heads,
        keys_new.reshape(row_count, head_count, HD),
        preferred_element_type=jnp.float32,
    ) / math.sqrt(HD)
    new_scores = jnp.where((visible == 1)[None, None, :], new_scores, jnp.float32(-1e30))
    scores = jnp.concatenate([cache_scores, new_scores], axis=2)
    row_max = jnp.max(scores, axis=2, keepdims=True)
    exponent = jnp.exp(scores - row_max)
    weights = (exponent / jnp.sum(exponent, axis=2, keepdims=True)).astype(jnp.bfloat16)
    mixed = jnp.einsum(
        "hqk,khd->qhd",
        weights[:, :, cache_span:],
        values_new.reshape(row_count, head_count, HD),
        preferred_element_type=jnp.float32,
    )
    mixed = mixed + jnp.einsum(
        "hqk,khd->qhd", weights[:, :, :cache_span], cache_values, preferred_element_type=jnp.float32
    )
    return mixed.reshape(row_count, head_count * HD).astype(jnp.bfloat16)


TP = ("x", "c")


def gather_tp(blocks):
    return lax.all_to_all(blocks, TP, split_axis=0, concat_axis=0, tiled=True)


def gather_two_stage(value):
    across = lax.all_to_all(
        spread(value, lax.axis_size("x")), "x", split_axis=0, concat_axis=0, tiled=True
    )
    both = lax.all_to_all(
        spread(across, lax.axis_size("c")), "c", split_axis=0, concat_axis=0, tiled=True
    )
    both = jnp.swapaxes(both, 0, 1)
    return both.reshape((-1,) + value.shape)


def spread(value, count):
    return jnp.broadcast_to(value[None], (count,) + value.shape)


def side_by_side(blocks):
    count, rows, width = blocks.shape
    return jnp.transpose(blocks, (1, 0, 2)).reshape(rows, count * width)


def on_device(
    tokens, norm_gain, input_weight, output_weight, cache_store, cache_length, placement, accept
):
    request_total = placement.shape[0]
    per_device = tokens.shape[0] // request_total
    local_width = tokens.shape[1]
    model_width = input_weight.shape[0]
    tp_count = model_width // local_width
    head_width = output_weight.shape[0]
    occupant = slot_owner(placement)
    device_index = lax.axis_index("req")
    my_request = occupant[device_index]
    my_length = cache_length[my_request]
    my_accept = accept.reshape(2, BLOCK, request_total)[:, :, my_request]
    block_weight = input_weight.reshape(tp_count, local_width, 3, -1)
    numbers = jnp.arange(request_total, dtype=jnp.int32)
    slot_pick = (placement[:, None] == numbers[None, :]).astype(tokens.dtype)

    by_slot = jnp.einsum(
        "jrf,rs->jsf",
        tokens.reshape(per_device, request_total, local_width),
        slot_pick,
        preferred_element_type=jnp.float32,
    ).astype(tokens.dtype)
    held = lax.all_to_all(by_slot, "req", split_axis=1, concat_axis=0, tiled=True).reshape(
        BLOCK, local_width
    )
    hidden = held.astype(jnp.float32)

    tp_index = lax.axis_index(TP)
    weight_blocks = jnp.transpose(
        output_weight.reshape(head_width, tp_count, local_width), (1, 0, 2)
    )
    arrived = gather_tp(jnp.concatenate([spread(held, tp_count), weight_blocks], axis=2))
    full = arrived[:, :, :local_width].astype(jnp.float32)
    column_weight = arrived[:, :, local_width:]
    gain_blocks = norm_gain.reshape(tp_count, 1, local_width)

    def branch_of(normed, visible):
        projected = jnp.einsum(
            "kpf,kfco->pco", normed, block_weight, preferred_element_type=jnp.float32
        ).astype(jnp.bfloat16)
        queries, keys_new, values_new = projected[:, 0], projected[:, 1], projected[:, 2]
        mixed = attend(queries, keys_new, values_new, cache_store[0], my_length, visible)
        return jnp.einsum(
            "kph,khf->pf", gather_two_stage(mixed), column_weight, preferred_element_type=jnp.float32
        )

    squares = jnp.sum(full * full, axis=(0, 2))[None, :, None]
    factor = lax.rsqrt(squares / model_width + epsilon)
    normed = (full * factor * gain_blocks).astype(jnp.bfloat16)
    first = hidden + branch_of(normed, my_accept[0])
    second = jnp.where(my_accept[0][:, None] == 1, first, hidden)
    partial = jnp.sum(second * second, axis=-1)
    squares = jnp.sum(gather_tp(spread(partial, tp_count)), axis=0)[:, None]
    factor = lax.rsqrt(squares / model_width + epsilon)
    my_gain = lax.dynamic_slice_in_dim(norm_gain, tp_index * local_width, local_width)
    normed_part = (second * factor * my_gain).astype(jnp.bfloat16)
    normed = gather_two_stage(normed_part)
    final = second + branch_of(normed, my_accept[1])

    both = jnp.concatenate([first, final], axis=1).reshape(BLOCK, 1, 2 * local_width)
    back = lax.all_to_all(both, "req", split_axis=0, concat_axis=1, tiled=True)[:, placement]
    back = back.reshape(per_device * request_total, 2 * local_width)
    return (back[:, :local_width], back[:, local_width:])


def solution(mesh):
    tp_size = mesh.shape["tp"]
    mesh = Mesh(
        mesh.devices.reshape(mesh.shape["req"], tp_size // 2, 2), ("req", "x", "c")
    )
    in_specs = (
        P("req", TP),
        P(),
        P(None, None, TP),
        P(TP, None),
        P("req", None, None, TP),
        P(),
        P(),
        P(),
    )
    out_specs = (P("req", TP), P("req", TP))
    return jax.shard_map(
        on_device, mesh=mesh, in_specs=in_specs, out_specs=out_specs, check_vma=False
    )
```

```python
import math

import jax
import jax.numpy as jnp
from jax import lax
from jax.sharding import Mesh, PartitionSpec as P

HD = 128
BLOCK = 256


epsilon = 1e-05


def slot_owner(placement):
    request_total = placement.shape[0]
    numbers = jnp.arange(request_total, dtype=jnp.int32)
    matches = placement[None, :] == numbers[:, None]
    return jnp.sum(jnp.where(matches, numbers[None, :], 0), axis=1)


def attend(queries, keys_new, values_new, cache_pair, length, visible):
    row_count = queries.shape[0]
    head_count = queries.shape[1] // HD
    cache_span = cache_pair.shape[1]
    query_heads = queries.reshape(row_count, head_count, HD)
    cache_keys = cache_pair[0].reshape(cache_span, head_count, HD)
    cache_values = cache_pair[1].reshape(cache_span, head_count, HD)
    cache_scores = jnp.einsum(
        "qhd,khd->hqk", query_heads, cache_keys, preferred_element_type=jnp.float32
    ) / math.sqrt(HD)
    inside = jnp.arange(cache_span, dtype=jnp.int32) < length
    cache_scores = jnp.where(inside[None, None, :], cache_scores, jnp.float32(-1e30))
    new_scores = jnp.einsum(
        "qhd,khd->hqk",
        query_heads,
        keys_new.reshape(row_count, head_count, HD),
        preferred_element_type=jnp.float32,
    ) / math.sqrt(HD)
    new_scores = jnp.where((visible == 1)[None, None, :], new_scores, jnp.float32(-1e30))
    scores = jnp.concatenate([cache_scores, new_scores], axis=2)
    row_max = jnp.max(scores, axis=2, keepdims=True)
    exponent = jnp.exp(scores - row_max)
    weights = (exponent / jnp.sum(exponent, axis=2, keepdims=True)).astype(jnp.bfloat16)
    mixed = jnp.einsum(
        "hqk,khd->qhd",
        weights[:, :, cache_span:],
        values_new.reshape(row_count, head_count, HD),
        preferred_element_type=jnp.float32,
    )
    mixed = mixed + jnp.einsum(
        "hqk,khd->qhd", weights[:, :, :cache_span], cache_values, preferred_element_type=jnp.float32
    )
    return mixed.reshape(row_count, head_count * HD).astype(jnp.bfloat16)


TP = ("x", "c")


def gather_tp(blocks):
    return lax.all_to_all(blocks, TP, split_axis=0, concat_axis=0, tiled=True)


def gather_two_stage(value):
    across = lax.all_to_all(
        spread(value, lax.axis_size("x")), "x", split_axis=0, concat_axis=0, tiled=True
    )
    both = lax.all_to_all(
        spread(across, lax.axis_size("c")), "c", split_axis=0, concat_axis=0, tiled=True
    )
    both = jnp.swapaxes(both, 0, 1)
    return both.reshape((-1,) + value.shape)


def spread(value, count):
    return jnp.broadcast_to(value[None], (count,) + value.shape)


def side_by_side(blocks):
    count, rows, width = blocks.shape
    return jnp.transpose(blocks, (1, 0, 2)).reshape(rows, count * width)


def on_device(
    tokens, norm_gain, input_weight, output_weight, cache_store, cache_length, placement, accept
):
    request_total = placement.shape[0]
    per_device = tokens.shape[0] // request_total
    local_width = tokens.shape[1]
    model_width = input_weight.shape[0]
    tp_count = model_width // local_width
    head_width = output_weight.shape[0]
    occupant = slot_owner(placement)
    device_index = lax.axis_index("req")
    my_request = occupant[device_index]
    my_length = cache_length[my_request]
    my_accept = accept.reshape(2, BLOCK, request_total)[:, :, my_request]
    block_weight = input_weight.reshape(tp_count, local_width, -1)
    numbers = jnp.arange(request_total, dtype=jnp.int32)
    slot_pick = (placement[:, None] == numbers[None, :]).astype(tokens.dtype)

    by_slot = jnp.einsum(
        "jrf,rs->jsf",
        tokens.reshape(per_device, request_total, local_width),
        slot_pick,
        preferred_element_type=jnp.float32,
    ).astype(tokens.dtype)
    held = lax.all_to_all(by_slot, "req", split_axis=1, concat_axis=0, tiled=True).reshape(
        BLOCK, local_width
    )
    hidden = held.astype(jnp.float32)

    tp_index = lax.axis_index(TP)
    weight_blocks = jnp.transpose(
        output_weight.reshape(head_width, tp_count, local_width), (1, 0, 2)
    )
    arrived = gather_tp(jnp.concatenate([spread(held, tp_count), weight_blocks], axis=2))
    full = arrived[:, :, :local_width].astype(jnp.float32)
    column_weight = arrived[:, :, local_width:]
    gain_blocks = norm_gain.reshape(tp_count, 1, local_width)

    def branch_of(normed, visible):
        projected = jnp.einsum(
            "kpf,kfo->po", normed, block_weight, preferred_element_type=jnp.float32
        ).astype(jnp.bfloat16)
        queries, keys_new, values_new = jnp.split(projected, 3, axis=1)
        mixed = attend(queries, keys_new, values_new, cache_store[0], my_length, visible)
        return jnp.einsum(
            "kph,khf->pf", gather_two_stage(mixed), column_weight, preferred_element_type=jnp.float32
        )

    squares = jnp.sum(full * full, axis=(0, 2))[None, :, None]
    factor = lax.rsqrt(squares / model_width + epsilon)
    normed = (full * factor * gain_blocks).astype(jnp.bfloat16)
    first = hidden + branch_of(normed, my_accept[0])
    second = jnp.where(my_accept[0][:, None] == 1, first, hidden)
    partial = jnp.sum(second * second, axis=-1)[None, :]
    parts = gather_two_stage(jnp.concatenate([second, partial], axis=0))
    squares = jnp.sum(parts[:, BLOCK, :], axis=0)[None, :, None]
    factor = lax.rsqrt(squares / model_width + epsilon)
    normed = (parts[:, :BLOCK, :] * factor * gain_blocks).astype(jnp.bfloat16)
    final = second + branch_of(normed, my_accept[1])

    both = jnp.concatenate([first, final], axis=1).reshape(BLOCK, 1, 2 * local_width)
    back = lax.all_to_all(both, "req", split_axis=0, concat_axis=1, tiled=True)[:, placement]
    back = back.reshape(per_device * request_total, 2 * local_width)
    return (back[:, :local_width], back[:, local_width:])


def solution(mesh):
    tp_size = mesh.shape["tp"]
    mesh = Mesh(
        mesh.devices.reshape(mesh.shape["req"], tp_size // 2, 2), ("req", "x", "c")
    )
    in_specs = (
        P("req", TP),
        P(),
        P(None, None, TP),
        P(TP, None),
        P("req", None, None, TP),
        P(),
        P(),
        P(),
    )
    out_specs = (P("req", TP), P("req", TP))
    return jax.shard_map(
        on_device, mesh=mesh, in_specs=in_specs, out_specs=out_specs, check_vma=False
    )
```

```python
import math

import jax
import jax.numpy as jnp
from jax import lax
from jax.sharding import Mesh, PartitionSpec as P

HD = 128
BLOCK = 256


epsilon = 1e-05


def slot_owner(placement):
    request_total = placement.shape[0]
    numbers = jnp.arange(request_total, dtype=jnp.int32)
    matches = placement[None, :] == numbers[:, None]
    return jnp.sum(jnp.where(matches, numbers[None, :], 0), axis=1)


def attend(queries, keys_new, values_new, cache_pair, length, visible):
    row_count = queries.shape[0]
    head_count = queries.shape[1] // HD
    cache_span = cache_pair.shape[1]
    query_heads = queries.reshape(row_count, head_count, HD)
    cache_keys = cache_pair[0].reshape(cache_span, head_count, HD)
    cache_values = cache_pair[1].reshape(cache_span, head_count, HD)
    cache_scores = jnp.einsum(
        "qhd,khd->hqk", query_heads, cache_keys, preferred_element_type=jnp.float32
    ) / math.sqrt(HD)
    inside = jnp.arange(cache_span, dtype=jnp.int32) < length
    cache_scores = jnp.where(inside[None, None, :], cache_scores, jnp.float32(-1e30))
    new_scores = jnp.einsum(
        "qhd,khd->hqk",
        query_heads,
        keys_new.reshape(row_count, head_count, HD),
        preferred_element_type=jnp.float32,
    ) / math.sqrt(HD)
    new_scores = jnp.where((visible == 1)[None, None, :], new_scores, jnp.float32(-1e30))
    scores = jnp.concatenate([cache_scores, new_scores], axis=2)
    row_max = jnp.max(scores, axis=2, keepdims=True)
    exponent = jnp.exp(scores - row_max)
    weights = (exponent / jnp.sum(exponent, axis=2, keepdims=True)).astype(jnp.bfloat16)
    mixed = jnp.einsum(
        "hqk,khd->qhd",
        weights[:, :, cache_span:],
        values_new.reshape(row_count, head_count, HD),
        preferred_element_type=jnp.float32,
    )
    mixed = mixed + jnp.einsum(
        "hqk,khd->qhd", weights[:, :, :cache_span], cache_values, preferred_element_type=jnp.float32
    )
    return mixed.reshape(row_count, head_count * HD).astype(jnp.bfloat16)


TP = ("x", "c")


def gather_tp(blocks):
    return lax.all_to_all(blocks, TP, split_axis=0, concat_axis=0, tiled=True)


def gather_two_stage(value):
    across = lax.all_to_all(
        spread(value, lax.axis_size("x")), "x", split_axis=0, concat_axis=0, tiled=True
    )
    both = lax.all_to_all(
        spread(across, lax.axis_size("c")), "c", split_axis=0, concat_axis=0, tiled=True
    )
    both = jnp.swapaxes(both, 0, 1)
    return both.reshape((-1,) + value.shape)


def spread(value, count):
    return jnp.broadcast_to(value[None], (count,) + value.shape)


def side_by_side(blocks):
    count, rows, width = blocks.shape
    return jnp.transpose(blocks, (1, 0, 2)).reshape(rows, count * width)


def on_device(
    tokens, norm_gain, input_weight, output_weight, cache_store, cache_length, placement, accept
):
    request_total = placement.shape[0]
    per_device = tokens.shape[0] // request_total
    local_width = tokens.shape[1]
    model_width = input_weight.shape[0]
    tp_count = model_width // local_width
    head_width = output_weight.shape[0]
    occupant = slot_owner(placement)
    device_index = lax.axis_index("req")
    my_request = occupant[device_index]
    my_length = cache_length[my_request]
    my_accept = accept.reshape(2, BLOCK, request_total)[:, :, my_request]
    block_weight = input_weight.reshape(tp_count, local_width, -1)
    numbers = jnp.arange(request_total, dtype=jnp.int32)
    slot_pick = (placement[:, None] == numbers[None, :]).astype(tokens.dtype)

    by_slot = jnp.einsum(
        "jrf,rs->sjf",
        tokens.reshape(per_device, request_total, local_width),
        slot_pick,
        preferred_element_type=jnp.float32,
    ).astype(tokens.dtype)
    held = lax.all_to_all(by_slot, "req", split_axis=0, concat_axis=0, tiled=True).reshape(
        BLOCK, local_width
    )
    hidden = held.astype(jnp.float32)

    tp_index = lax.axis_index(TP)
    weight_blocks = jnp.transpose(
        output_weight.reshape(head_width, tp_count, local_width), (1, 0, 2)
    )
    arrived = gather_tp(jnp.concatenate([spread(held, tp_count), weight_blocks], axis=2))
    full = arrived[:, :, :local_width].astype(jnp.float32)
    column_weight = arrived[:, :, local_width:]
    gain_blocks = norm_gain.reshape(tp_count, 1, local_width)

    def branch_of(normed, visible):
        projected = jnp.einsum(
            "kpf,kfo->po", normed, block_weight, preferred_element_type=jnp.float32
        ).astype(jnp.bfloat16)
        queries, keys_new, values_new = jnp.split(projected, 3, axis=1)
        mixed = attend(queries, keys_new, values_new, cache_store[0], my_length, visible)
        return jnp.einsum(
            "kph,khf->pf", gather_two_stage(mixed), column_weight, preferred_element_type=jnp.float32
        )

    squares = jnp.sum(full * full, axis=(0, 2))[None, :, None]
    factor = lax.rsqrt(squares / model_width + epsilon)
    normed = (full * factor * gain_blocks).astype(jnp.bfloat16)
    first = hidden + branch_of(normed, my_accept[0])
    second = jnp.where(my_accept[0][:, None] == 1, first, hidden)
    partial = jnp.sum(second * second, axis=-1)
    squares = jnp.sum(gather_tp(spread(partial, tp_count)), axis=0)[:, None]
    factor = lax.rsqrt(squares / model_width + epsilon)
    my_gain = lax.dynamic_slice_in_dim(norm_gain, tp_index * local_width, local_width)
    normed_part = (second * factor * my_gain).astype(jnp.bfloat16)
    normed = gather_two_stage(normed_part)
    final = second + branch_of(normed, my_accept[1])

    both = jnp.concatenate([first, final], axis=1).reshape(BLOCK, 1, 2 * local_width)
    back = lax.all_to_all(both, "req", split_axis=0, concat_axis=1, tiled=True)[:, placement]
    back = back.reshape(per_device * request_total, 2 * local_width)
    return (back[:, :local_width], back[:, local_width:])


def solution(mesh):
    tp_size = mesh.shape["tp"]
    mesh = Mesh(
        mesh.devices.reshape(mesh.shape["req"], tp_size // 2, 2), ("req", "x", "c")
    )
    in_specs = (
        P("req", TP),
        P(),
        P(None, None, TP),
        P(TP, None),
        P("req", None, None, TP),
        P(),
        P(),
        P(),
    )
    out_specs = (P("req", TP), P("req", TP))
    return jax.shard_map(
        on_device, mesh=mesh, in_specs=in_specs, out_specs=out_specs, check_vma=False
    )
```

```python
import math

import jax
import jax.numpy as jnp
from jax import lax
from jax.sharding import Mesh, PartitionSpec as P

HD = 128
BLOCK = 256


epsilon = 1e-05


def slot_owner(placement):
    request_total = placement.shape[0]
    numbers = jnp.arange(request_total, dtype=jnp.int32)
    matches = placement[None, :] == numbers[:, None]
    return jnp.sum(jnp.where(matches, numbers[None, :], 0), axis=1)


def attend(queries, keys_new, values_new, cache_pair, length, visible):
    row_count = queries.shape[0]
    head_count = queries.shape[1] // HD
    cache_span = cache_pair.shape[1]
    query_heads = queries.reshape(row_count, head_count, HD)
    cache_keys = cache_pair[0].reshape(cache_span, head_count, HD)
    cache_values = cache_pair[1].reshape(cache_span, head_count, HD)
    cache_scores = jnp.einsum(
        "qhd,khd->hqk", query_heads, cache_keys, preferred_element_type=jnp.float32
    ) / math.sqrt(HD)
    inside = jnp.arange(cache_span, dtype=jnp.int32) < length
    cache_scores = jnp.where(inside[None, None, :], cache_scores, jnp.float32(-1e30))
    new_scores = jnp.einsum(
        "qhd,khd->hqk",
        query_heads,
        keys_new.reshape(row_count, head_count, HD),
        preferred_element_type=jnp.float32,
    ) / math.sqrt(HD)
    new_scores = jnp.where((visible == 1)[None, None, :], new_scores, jnp.float32(-1e30))
    scores = jnp.concatenate([cache_scores, new_scores], axis=2)
    row_max = jnp.max(scores, axis=2, keepdims=True)
    exponent = jnp.exp(scores - row_max)
    weights = (exponent / jnp.sum(exponent, axis=2, keepdims=True)).astype(jnp.bfloat16)
    mixed = jnp.einsum(
        "hqk,khd->qhd",
        weights[:, :, cache_span:],
        values_new.reshape(row_count, head_count, HD),
        preferred_element_type=jnp.float32,
    )
    mixed = mixed + jnp.einsum(
        "hqk,khd->qhd", weights[:, :, :cache_span], cache_values, preferred_element_type=jnp.float32
    )
    return mixed.reshape(row_count, head_count * HD).astype(jnp.bfloat16)


TP = ("x", "c")


def gather_tp(blocks):
    return lax.all_to_all(blocks, TP, split_axis=0, concat_axis=0, tiled=True)


def gather_two_stage(value):
    across = lax.all_to_all(
        spread(value, lax.axis_size("x")), "x", split_axis=0, concat_axis=0, tiled=True
    )
    both = lax.all_to_all(
        spread(across, lax.axis_size("c")), "c", split_axis=0, concat_axis=0, tiled=True
    )
    both = jnp.swapaxes(both, 0, 1)
    return both.reshape((-1,) + value.shape)


def spread(value, count):
    return jnp.broadcast_to(value[None], (count,) + value.shape)


def side_by_side(blocks):
    count, rows, width = blocks.shape
    return jnp.transpose(blocks, (1, 0, 2)).reshape(rows, count * width)


def on_device(
    tokens, norm_gain, input_weight, output_weight, cache_store, cache_length, placement, accept
):
    request_total = placement.shape[0]
    per_device = tokens.shape[0] // request_total
    local_width = tokens.shape[1]
    model_width = input_weight.shape[0]
    tp_count = model_width // local_width
    head_width = output_weight.shape[0]
    occupant = slot_owner(placement)
    device_index = lax.axis_index("req")
    my_request = occupant[device_index]
    my_length = cache_length[my_request]
    my_accept = accept.reshape(2, BLOCK, request_total)[:, :, my_request]
    block_weight = input_weight.reshape(tp_count, local_width, -1)
    numbers = jnp.arange(request_total, dtype=jnp.int32)
    slot_pick = (placement[:, None] == numbers[None, :]).astype(tokens.dtype)

    by_slot = jnp.einsum(
        "jrf,rs->sjf",
        tokens.reshape(per_device, request_total, local_width),
        slot_pick,
        preferred_element_type=jnp.float32,
    ).astype(tokens.dtype)
    held = lax.all_to_all(by_slot, "req", split_axis=0, concat_axis=0, tiled=True).reshape(
        BLOCK, local_width
    )
    hidden = held.astype(jnp.float32)

    tp_index = lax.axis_index(TP)
    weight_blocks = jnp.transpose(
        output_weight.reshape(head_width, tp_count, local_width), (1, 0, 2)
    )
    arrived = gather_tp(jnp.concatenate([spread(held, tp_count), weight_blocks], axis=2))
    full = arrived[:, :, :local_width].astype(jnp.float32)
    column_weight = arrived[:, :, local_width:]
    gain_blocks = norm_gain.reshape(tp_count, 1, local_width)

    def branch_of(normed, visible):
        projected = jnp.einsum(
            "kpf,kfo->po", normed, block_weight, preferred_element_type=jnp.float32
        ).astype(jnp.bfloat16)
        queries, keys_new, values_new = jnp.split(projected, 3, axis=1)
        mixed = attend(queries, keys_new, values_new, cache_store[0], my_length, visible)
        return jnp.einsum(
            "kph,khf->pf", gather_two_stage(mixed), column_weight, preferred_element_type=jnp.float32
        )

    squares = jnp.sum(full * full, axis=(0, 2))[None, :, None]
    factor = lax.rsqrt(squares / model_width + epsilon)
    normed = lax.optimization_barrier((full * factor * gain_blocks).astype(jnp.bfloat16))
    first = hidden + branch_of(normed, my_accept[0])
    second = jnp.where(my_accept[0][:, None] == 1, first, hidden)
    partial = jnp.sum(second * second, axis=-1)
    squares = jnp.sum(gather_tp(spread(partial, tp_count)), axis=0)[:, None]
    factor = lax.rsqrt(squares / model_width + epsilon)
    my_gain = lax.dynamic_slice_in_dim(norm_gain, tp_index * local_width, local_width)
    normed_part = (second * factor * my_gain).astype(jnp.bfloat16)
    normed = gather_two_stage(normed_part)
    final = second + branch_of(normed, my_accept[1])

    both = jnp.concatenate([first, final], axis=1).reshape(BLOCK, 1, 2 * local_width)
    back = lax.all_to_all(both, "req", split_axis=0, concat_axis=1, tiled=True)[:, placement]
    back = back.reshape(per_device * request_total, 2 * local_width)
    return (back[:, :local_width], back[:, local_width:])


def solution(mesh):
    tp_size = mesh.shape["tp"]
    mesh = Mesh(
        mesh.devices.reshape(mesh.shape["req"], tp_size // 2, 2), ("req", "x", "c")
    )
    in_specs = (
        P("req", TP),
        P(),
        P(None, None, TP),
        P(TP, None),
        P("req", None, None, TP),
        P(),
        P(),
        P(),
    )
    out_specs = (P("req", TP), P("req", TP))
    return jax.shard_map(
        on_device, mesh=mesh, in_specs=in_specs, out_specs=out_specs, check_vma=False
    )
```

```python
import math

import jax
import jax.numpy as jnp
from jax import lax
from jax.sharding import Mesh, PartitionSpec as P

HD = 128
BLOCK = 256


epsilon = 1e-05


def slot_owner(placement):
    request_total = placement.shape[0]
    numbers = jnp.arange(request_total, dtype=jnp.int32)
    matches = placement[None, :] == numbers[:, None]
    return jnp.sum(jnp.where(matches, numbers[None, :], 0), axis=1)


def attend(queries, keys_new, values_new, cache_pair, length, visible):
    row_count = queries.shape[0]
    head_count = queries.shape[1] // HD
    cache_span = cache_pair.shape[1]
    query_heads = queries.reshape(row_count, head_count, HD)
    cache_keys = cache_pair[0].reshape(cache_span, head_count, HD)
    cache_values = cache_pair[1].reshape(cache_span, head_count, HD)
    cache_scores = jnp.einsum(
        "qhd,khd->hqk", query_heads, cache_keys, preferred_element_type=jnp.float32
    ) / math.sqrt(HD)
    inside = jnp.arange(cache_span, dtype=jnp.int32) < length
    cache_scores = jnp.where(inside[None, None, :], cache_scores, jnp.float32(-1e30))
    new_scores = jnp.einsum(
        "qhd,khd->hqk",
        query_heads,
        keys_new.reshape(row_count, head_count, HD),
        preferred_element_type=jnp.float32,
    ) / math.sqrt(HD)
    new_scores = jnp.where((visible == 1)[None, None, :], new_scores, jnp.float32(-1e30))
    scores = jnp.concatenate([cache_scores, new_scores], axis=2)
    row_max = jnp.max(scores, axis=2, keepdims=True)
    exponent = jnp.exp(scores - row_max)
    weights = (exponent / jnp.sum(exponent, axis=2, keepdims=True)).astype(jnp.bfloat16)
    mixed = jnp.einsum(
        "hqk,khd->qhd",
        weights[:, :, cache_span:],
        values_new.reshape(row_count, head_count, HD),
        preferred_element_type=jnp.float32,
    )
    mixed = mixed + jnp.einsum(
        "hqk,khd->qhd", weights[:, :, :cache_span], cache_values, preferred_element_type=jnp.float32
    )
    return mixed.reshape(row_count, head_count * HD).astype(jnp.bfloat16)


TP = ("x", "c")


def gather_tp(blocks):
    return lax.all_to_all(blocks, TP, split_axis=0, concat_axis=0, tiled=True)


def gather_two_stage(value):
    across = lax.all_to_all(
        spread(value, lax.axis_size("x")), "x", split_axis=0, concat_axis=0, tiled=True
    )
    both = lax.all_to_all(
        spread(across, lax.axis_size("c")), "c", split_axis=0, concat_axis=0, tiled=True
    )
    both = jnp.swapaxes(both, 0, 1)
    return both.reshape((-1,) + value.shape)


def spread(value, count):
    return jnp.broadcast_to(value[None], (count,) + value.shape)


def side_by_side(blocks):
    count, rows, width = blocks.shape
    return jnp.transpose(blocks, (1, 0, 2)).reshape(rows, count * width)


def on_device(
    tokens, norm_gain, input_weight, output_weight, cache_store, cache_length, placement, accept
):
    request_total = placement.shape[0]
    per_device = tokens.shape[0] // request_total
    local_width = tokens.shape[1]
    model_width = input_weight.shape[0]
    tp_count = model_width // local_width
    head_width = output_weight.shape[0]
    occupant = slot_owner(placement)
    device_index = lax.axis_index("req")
    my_request = occupant[device_index]
    my_length = cache_length[my_request]
    my_accept = accept.reshape(2, BLOCK, request_total)[:, :, my_request]
    block_weight = input_weight.reshape(tp_count, local_width, -1)
    numbers = jnp.arange(request_total, dtype=jnp.int32)
    slot_pick = (placement[:, None] == numbers[None, :]).astype(tokens.dtype)

    by_slot = jnp.einsum(
        "jrf,rs->sjf",
        tokens.reshape(per_device, request_total, local_width),
        slot_pick,
        preferred_element_type=jnp.float32,
    ).astype(tokens.dtype)
    held = lax.all_to_all(by_slot, "req", split_axis=0, concat_axis=0, tiled=True).reshape(
        BLOCK, local_width
    )
    hidden = held.astype(jnp.float32)

    tp_index = lax.axis_index(TP)
    weight_blocks = jnp.transpose(
        output_weight.reshape(head_width, tp_count, local_width), (1, 0, 2)
    )
    arrived = gather_tp(jnp.concatenate([spread(held, tp_count), weight_blocks], axis=2))
    full = arrived[:, :, :local_width].astype(jnp.float32)
    column_weight = arrived[:, :, local_width:]
    gain_blocks = norm_gain.reshape(tp_count, 1, local_width)

    def branch_of(normed, visible):
        if normed.ndim == 2:
            flat = block_weight.reshape(model_width, -1)
            projected = jnp.dot(normed, flat, preferred_element_type=jnp.float32)
        else:
            projected = jnp.einsum(
                "kpf,kfo->po", normed, block_weight, preferred_element_type=jnp.float32
            )
        projected = projected.astype(jnp.bfloat16)
        queries, keys_new, values_new = jnp.split(projected, 3, axis=1)
        mixed = attend(queries, keys_new, values_new, cache_store[0], my_length, visible)
        return jnp.einsum(
            "kph,khf->pf", gather_two_stage(mixed), column_weight, preferred_element_type=jnp.float32
        )

    squares = jnp.sum(full * full, axis=(0, 2))[None, :, None]
    factor = lax.rsqrt(squares / model_width + epsilon)
    normed = (full * factor * gain_blocks).astype(jnp.bfloat16)
    first = hidden + branch_of(side_by_side(normed), my_accept[0])
    second = jnp.where(my_accept[0][:, None] == 1, first, hidden)
    partial = jnp.sum(second * second, axis=-1)
    squares = jnp.sum(gather_tp(spread(partial, tp_count)), axis=0)[:, None]
    factor = lax.rsqrt(squares / model_width + epsilon)
    my_gain = lax.dynamic_slice_in_dim(norm_gain, tp_index * local_width, local_width)
    normed_part = (second * factor * my_gain).astype(jnp.bfloat16)
    normed = gather_two_stage(normed_part)
    final = second + branch_of(normed, my_accept[1])

    both = jnp.concatenate([first, final], axis=1).reshape(BLOCK, 1, 2 * local_width)
    back = lax.all_to_all(both, "req", split_axis=0, concat_axis=1, tiled=True)[:, placement]
    back = back.reshape(per_device * request_total, 2 * local_width)
    return (back[:, :local_width], back[:, local_width:])


def solution(mesh):
    tp_size = mesh.shape["tp"]
    mesh = Mesh(
        mesh.devices.reshape(mesh.shape["req"], tp_size // 2, 2), ("req", "x", "c")
    )
    in_specs = (
        P("req", TP),
        P(),
        P(None, None, TP),
        P(TP, None),
        P("req", None, None, TP),
        P(),
        P(),
        P(),
    )
    out_specs = (P("req", TP), P("req", TP))
    return jax.shard_map(
        on_device, mesh=mesh, in_specs=in_specs, out_specs=out_specs, check_vma=False
    )
```
